512 devices in a mesh: row: 16 (over y_lo, x), col: 32 (over z, y_hi, core).
Axes of the slice: x: 4, y: 8 (y_hi: 2, y_lo: 4; y = y_hi * 4 + y_lo), z: 8, core: 2. Of those that a mesh axis runs over, the one named last changes fastest.
Arguments:
- precond: float32 [8, 8192, 8192], P(None, 'row', 'col'), may hold values from -6 to 6
- out_factors: bfloat16 [1536, 8192], P('col', 'row'), may hold values from -6 to 6
- in_factors: bfloat16 [1536, 8192], P('row', 'col'), may hold values from -6 to 6
- token_mask: int32 [1536], replicated, may hold values 0 or 1
- seq_ids: int32 [1536], replicated, may hold values from 0 to 3, never falling along the last dimension, each value on 1 to 576 neighbouring positions
- query_ids: int32 [8], replicated, may hold values from 0 to 7, each once
Outputs:
- scores: float32 [8, 4], replicated
The draws below stay inside these ranges and needn't reach their ends.
Inputs may be any that keep to these rules, and one draw needn't show every extreme that they name: seq_ids never falls along the tokens; each sequence has 1 to 576 tokens. query_ids names each query once.
All inputs are finite; a program needn't handle non-finite values.
Results may differ from the reference program's by a relative error of at most 0.0003.
Values may be sent and summed in bfloat16 or wider, within the bound.
No kernel may reach another device: no remote copies, remote signals or barrier semaphores. Data moves between devices by JAX's collectives and lax.ppermute only.
A program may use at most 64 MiB of HBM per device.

```python
import math
import jax
import jax.numpy as jnp
import numpy as np
from jax import lax

DOUT = 8192
DIN = 8192
QUERIES = 8
SEQ = 4
LEN = 384
TOKENS = 1536
MOST = 576


def with_ends(array, rng, smallest, high):
    shape = array.shape
    spot = [jax.random.randint(jax.random.fold_in(rng, axis), (), 0, shape[axis]) for axis in range(len(shape))]
    array = array.at[tuple(spot)].set(smallest)
    longest = shape.index(max(shape))
    spot[longest] = (spot[longest] + 1) % shape[longest]
    return array.at[tuple(spot)].set(high)


def levels(rng, shape, split, smallest, top_value):
    def one(axis_at, parts):
        heights = jax.random.uniform(jax.random.fold_in(jax.random.fold_in(rng, 6), axis_at), (parts,), jnp.float32, smallest / len(split), top_value / len(split))
        return jnp.repeat(jnp.exp(heights), shape[axis_at] // parts).reshape((-1,) + (1,) * (len(shape) - axis_at - 1))

    level = one(*split[0])
    for cut in split[1:]:
        level = level * one(*cut)
    return level


def split_up(number_of, total, limit, lean):
    loads = [(1 << 20) // math.isqrt(grade ** lean) + 1 for grade in range(2, number_of + 1)]
    spare, counts = total - limit - (number_of - 1), [1] * (number_of - 1)
    while spare > 0:
        free = [i for i in range(number_of - 1) if counts[i] < limit]
        pool, left = sum([loads[i] for i in free]), spare
        for i in free:
            addition = min(limit - counts[i], max(1, left * loads[i] // pool), spare)
            counts[i] = counts[i] + addition
            spare = spare - addition
    return np.array([limit] + counts)


def ragged_sizes(rng, number_of, total, limit, skew):
    if number_of == 2:
        one = jax.random.randint(rng, (), max(1, total - limit), min(limit, total - 1) + 1)
        return jnp.stack([one, total - one])
    tallies = jnp.asarray(split_up(number_of, total, limit, skew), jnp.int32)
    pairs = (number_of - 1) // 2
    donor, sink = tallies[1:1 + 2 * pairs:2], tallies[2:2 + 2 * pairs:2]
    room = jnp.minimum(donor - 1, limit - sink)
    shifted = jax.random.randint(jax.random.fold_in(rng, 1), (pairs,), 0, 1 << 20) % (room + 1)
    tallies = tallies.at[1:1 + 2 * pairs:2].set(donor - shifted).at[2:2 + 2 * pairs:2].set(sink + shifted)
    return tallies[jax.random.permutation(jax.random.fold_in(rng, 2), number_of)]


def gaussian(stream_key, dims, deviation, bound, pieces=(), kind=jnp.bfloat16):
    factor_of = levels(stream_key, dims, pieces, -0.22, 0.18) if pieces else 1.0
    drawn = jax.random.normal(stream_key, dims, jnp.float32) * deviation * factor_of
    return jnp.minimum(jnp.maximum(drawn, -bound), bound).astype(kind)


def setup_inputs(seed: int = 0) -> dict:
    keys = jax.random.split(jax.random.key(seed), 7)
    return {
        "precond": gaussian(keys[0], (QUERIES, DOUT, DIN), 1.0, 6.0, ((1, 16), (2, 32)), jnp.float32),
        "out_factors": gaussian(keys[1], (TOKENS, DOUT), 1.0, 6.0, ((0, 32), (1, 16))),
        "in_factors": gaussian(keys[2], (TOKENS, DIN), 1.0, 6.0, ((0, 16), (1, 32))),
        "token_mask": with_ends((jax.random.randint(keys[3], (TOKENS,), 0, 4) < 3).astype(jnp.int32), jax.random.fold_in(keys[3], 1), 0, 1),
        "seq_ids": jnp.searchsorted(jnp.cumsum(ragged_sizes(keys[4], SEQ, TOKENS, MOST, 0)), jnp.arange(TOKENS), side="right").astype(jnp.int32),
        "query_ids": jax.random.permutation(keys[5], QUERIES).astype(jnp.int32),
    }


def reference(precond, out_factors, in_factors, token_mask, seq_ids, query_ids):
    weight = token_mask.astype(jnp.float32)[:, None] * (seq_ids[:, None] == jnp.arange(SEQ, dtype=jnp.int32)[None, :]).astype(jnp.float32)
    out_wide = out_factors.astype(jnp.float32)
    in_wide = in_factors.astype(jnp.float32)

    def one_query(query_grad):
        mapped = jnp.dot(in_wide, query_grad.T, precision=lax.Precision.HIGHEST)
        per_token = lax.optimization_barrier(jnp.sum(mapped * out_wide, axis=1))
        return jnp.dot(per_token, weight, precision=lax.Precision.HIGHEST)
    raw = lax.map(one_query, precond)
    select = (query_ids[:, None] == jnp.arange(QUERIES, dtype=jnp.int32)[None, :]).astype(jnp.float32)
    scale = 1.0 / math.sqrt(DOUT * DIN * LEN)
    return jnp.dot(select, raw, precision=lax.Precision.HIGHEST) * scale
```

```python
import math

import jax
import jax.numpy as jnp
from jax import lax
from jax.sharding import PartitionSpec as P

DOUT = 8192
DIN = 8192
SEQ = 4
LEN = 384
GATHER = "a2a"
FINAL = "a2a2"


def _gather(x, axis, size):
    if GATHER == "ag":
        return lax.all_gather(x, axis, axis=0, tiled=True)
    sent = jnp.broadcast_to(x[None], (size,) + x.shape)
    got = lax.all_to_all(sent, axis, 0, 0, tiled=True)
    return got.reshape((size * x.shape[0],) + x.shape[1:])


def _sum_over(x, axes, size):
    sent = jnp.broadcast_to(x[None], (size,) + x.shape)
    return lax.all_to_all(sent, axes, 0, 0, tiled=True).sum(0)


def shards(precond, out_factors, in_factors, token_mask, seq_ids, query_ids):
    num_queries = precond.shape[0]
    rows = lax.axis_size("row")
    cols = lax.axis_size("col")

    out_all = _gather(out_factors, "col", cols)
    in_all = _gather(in_factors, "row", rows)

    weight = token_mask.astype(jnp.float32)[:, None] * (
        seq_ids[:, None] == jnp.arange(SEQ, dtype=jnp.int32)[None, :]
    ).astype(jnp.float32)
    weighted = (weight.T[:, :, None] * out_all.astype(jnp.float32)[None]).astype(jnp.bfloat16)
    grad = lax.dot_general(
        weighted, in_all, (((1,), (0,)), ((), ())), preferred_element_type=jnp.float32
    )
    partial = lax.dot_general(
        precond, grad, (((1, 2), (1, 2)), ((), ())), precision=lax.Precision.HIGHEST
    )

    if FINAL == "psum":
        summed = lax.psum(partial, ("row", "col"))
    elif FINAL == "a2a1":
        summed = _sum_over(partial, ("row", "col"), rows * cols)
    else:
        summed = _sum_over(_sum_over(partial, "row", rows), "col", cols)

    select = (query_ids[:, None] == jnp.arange(num_queries, dtype=jnp.int32)[None, :]).astype(
        jnp.float32
    )
    scale = 1.0 / math.sqrt(DOUT * DIN * LEN)
    return jnp.dot(select, summed, precision=lax.Precision.HIGHEST) * scale


def solution(mesh):
    placed = (P(None, "row", "col"), P("col", "row"), P("row", "col"), P(), P(), P())
    return jax.shard_map(shards, mesh=mesh, in_specs=placed, out_specs=P(), check_vma=False)
```

```python
import math

import jax
import jax.numpy as jnp
from jax import lax
from jax.sharding import Mesh, PartitionSpec as P

DOUT = 8192
DIN = 8192
SEQ = 4
LEN = 384
GATHER = "a2a"


def _gather(x, axis, size):
    if GATHER == "ag":
        return lax.all_gather(x, axis, axis=0, tiled=True)
    sent = jnp.broadcast_to(x[None], (size,) + x.shape)
    got = lax.all_to_all(sent, axis, 0, 0, tiled=True)
    return got.reshape((size * x.shape[0],) + x.shape[1:])


def _sum_over(x, axes, size):
    sent = jnp.broadcast_to(x[None], (size,) + x.shape)
    return lax.all_to_all(sent, axes, 0, 0, tiled=True).sum(0)


def shards(precond, out_factors, in_factors, token_mask, seq_ids, query_ids):
    num_queries = precond.shape[0]
    rows = lax.axis_size("row")
    cols = lax.axis_size("cg") * lax.axis_size("cc")

    groups = lax.axis_size("cg")
    cores = lax.axis_size("cc")
    core = lax.axis_index("cc")
    same = _gather(out_factors, "cg", groups).reshape((groups, 1) + out_factors.shape)
    other = lax.ppermute(same, "cc", [(0, 1), (1, 0)])
    out_all = jnp.concatenate([same, other], axis=1).reshape((-1, out_factors.shape[1]))
    in_all = _gather(in_factors, "row", rows)

    def in_our_order(x):
        y = x.reshape((groups, cores, x.shape[0] // (groups * cores)) + x.shape[1:])
        return jnp.where(core == 0, y, y[:, ::-1]).reshape(x.shape)

    in_all = in_our_order(in_all)
    weight = token_mask.astype(jnp.float32)[:, None] * (
        seq_ids[:, None] == jnp.arange(SEQ, dtype=jnp.int32)[None, :]
    ).astype(jnp.float32)
    weight = in_our_order(weight)
    weighted = weight.T.astype(jnp.bfloat16)[:, :, None] * in_all[None]
    grad = jnp.einsum("ti,stj->sij", out_all, weighted, preferred_element_type=jnp.float32)
    partial = jnp.sum(precond[:, None] * grad[None], axis=(2, 3))

    summed = _sum_over(_sum_over(partial, "row", rows), ("cg", "cc"), cols)

    select = (query_ids[:, None] == jnp.arange(num_queries, dtype=jnp.int32)[None, :]).astype(
        jnp.float32
    )
    scale = 1.0 / math.sqrt(DOUT * DIN * LEN)
    return jnp.dot(select, summed, precision=lax.Precision.HIGHEST) * scale


def solution(mesh):
    rows, cols = mesh.devices.shape
    split = Mesh(mesh.devices.reshape(rows, cols // 2, 2), ("row", "cg", "cc"))
    col = ("cg", "cc")
    placed = (P(None, "row", col), P(col, "row"), P("row", col), P(), P(), P())
    return jax.shard_map(shards, mesh=split, in_specs=placed, out_specs=P(), check_vma=False)
```

```python
import math

import jax
import jax.numpy as jnp
from jax import lax
from jax.sharding import Mesh, PartitionSpec as P

DOUT = 8192
DIN = 8192
SEQ = 4
LEN = 384
GATHER = "a2a"


def _gather(x, axis, size):
    if GATHER == "ag":
        return lax.all_gather(x, axis, axis=0, tiled=True)
    sent = jnp.broadcast_to(x[None], (size,) + x.shape)
    got = lax.all_to_all(sent, axis, 0, 0, tiled=True)
    return got.reshape((size * x.shape[0],) + x.shape[1:])


def _sum_over(x, axes, size):
    sent = jnp.broadcast_to(x[None], (size,) + x.shape)
    return lax.all_to_all(sent, axes, 0, 0, tiled=True).sum(0)


def shards(precond, out_factors, in_factors, token_mask, seq_ids, query_ids):
    num_queries = precond.shape[0]
    rows = lax.axis_size("row")
    cols = lax.axis_size("cg") * lax.axis_size("cc")

    groups = lax.axis_size("cg")
    cores = lax.axis_size("cc")
    core = lax.axis_index("cc")
    same = _gather(out_factors, "cg", groups).reshape((groups, 1) + out_factors.shape)
    other = lax.ppermute(same, "cc", [(0, 1), (1, 0)])
    out_all = jnp.concatenate([same, other], axis=1).reshape((-1, out_factors.shape[1]))
    in_all = _gather(in_factors, "row", rows)

    def in_our_order(x):
        y = x.reshape((groups, cores, x.shape[0] // (groups * cores)) + x.shape[1:])
        return jnp.where(core == 0, y, y[:, ::-1]).reshape(x.shape)

    in_all = in_our_order(in_all)
    weight = token_mask.astype(jnp.float32)[:, None] * (
        seq_ids[:, None] == jnp.arange(SEQ, dtype=jnp.int32)[None, :]
    ).astype(jnp.float32)
    weight = in_our_order(weight)
    weighted = weight.T.astype(jnp.bfloat16)[:, :, None] * out_all[None]
    grad = jnp.einsum("sti,tj->sij", weighted, in_all, preferred_element_type=jnp.float32)
    partial = jnp.sum(precond[:, None] * grad[None], axis=(2, 3))

    summed = _sum_over(_sum_over(partial, ("row", "cc"), rows * cores), "cg", groups)

    select = (query_ids[:, None] == jnp.arange(num_queries, dtype=jnp.int32)[None, :]).astype(
        jnp.float32
    )
    scale = 1.0 / math.sqrt(DOUT * DIN * LEN)
    return jnp.dot(select, summed, precision=lax.Precision.HIGHEST) * scale


def solution(mesh):
    rows, cols = mesh.devices.shape
    split = Mesh(mesh.devices.reshape(rows, cols // 2, 2), ("row", "cg", "cc"))
    col = ("cg", "cc")
    placed = (P(None, "row", col), P(col, "row"), P("row", col), P(), P(), P())
    return jax.shard_map(shards, mesh=split, in_specs=placed, out_specs=P(), check_vma=False)
```

```python
import math

import jax
import jax.numpy as jnp
from jax import lax
from jax.sharding import Mesh, PartitionSpec as P

DOUT = 8192
DIN = 8192
SEQ = 4
LEN = 384
GATHER = "a2a"


def _gather(x, axis, size):
    if GATHER == "ag":
        return lax.all_gather(x, axis, axis=0, tiled=True)
    sent = jnp.broadcast_to(x[None], (size,) + x.shape)
    got = lax.all_to_all(sent, axis, 0, 0, tiled=True)
    return got.reshape((size * x.shape[0],) + x.shape[1:])


def _sum_over(x, axes, size):
    sent = jnp.broadcast_to(x[None], (size,) + x.shape)
    return lax.all_to_all(sent, axes, 0, 0, tiled=True).sum(0)


def shards(precond, out_factors, in_factors, token_mask, seq_ids, query_ids):
    num_queries = precond.shape[0]
    rows = lax.axis_size("row")
    cols = lax.axis_size("cz") * lax.axis_size("cy") * lax.axis_size("cc")

    groups = lax.axis_size("cz") * lax.axis_size("cy")
    cores = lax.axis_size("cc")
    core = lax.axis_index("cc")
    same = _gather(out_factors, ("cz", "cy"), groups).reshape((groups, 1) + out_factors.shape)
    other = lax.ppermute(same, "cc", [(0, 1), (1, 0)])
    out_all = jnp.concatenate([same, other], axis=1).reshape((-1, out_factors.shape[1]))
    in_all = _gather(in_factors, "row", rows)

    def in_our_order(x):
        y = x.reshape((groups, cores, x.shape[0] // (groups * cores)) + x.shape[1:])
        return jnp.where(core == 0, y, y[:, ::-1]).reshape(x.shape)

    in_all = in_our_order(in_all)
    weight = token_mask.astype(jnp.float32)[:, None] * (
        seq_ids[:, None] == jnp.arange(SEQ, dtype=jnp.int32)[None, :]
    ).astype(jnp.float32)
    weight = in_our_order(weight)
    weighted = weight.T.astype(jnp.bfloat16)[:, :, None] * out_all[None]
    grad = jnp.einsum("sti,tj->sij", weighted, in_all, preferred_element_type=jnp.float32)
    partial = jnp.sum(precond[:, None] * grad[None], axis=(2, 3))

    near = rows * cores * lax.axis_size("cy")
    summed = _sum_over(_sum_over(partial, ("row", "cy", "cc"), near), "cz", lax.axis_size("cz"))

    select = (query_ids[:, None] == jnp.arange(num_queries, dtype=jnp.int32)[None, :]).astype(
        jnp.float32
    )
    scale = 1.0 / math.sqrt(DOUT * DIN * LEN)
    return jnp.dot(select, summed, precision=lax.Precision.HIGHEST) * scale


def solution(mesh):
    rows, cols = mesh.devices.shape
    split = Mesh(mesh.devices.reshape(rows, cols // 4, 2, 2), ("row", "cz", "cy", "cc"))
    col = ("cz", "cy", "cc")
    placed = (P(None, "row", col), P(col, "row"), P("row", col), P(), P(), P())
    return jax.shard_map(shards, mesh=split, in_specs=placed, out_specs=P(), check_vma=False)
```

```python
import math

import jax
import jax.numpy as jnp
from jax import lax
from jax.sharding import Mesh, PartitionSpec as P

DOUT = 8192
DIN = 8192
SEQ = 4
LEN = 384
GATHER = "a2a"


def _gather(x, axis, size):
    if GATHER == "ag":
        return lax.all_gather(x, axis, axis=0, tiled=True)
    sent = jnp.broadcast_to(x[None], (size,) + x.shape)
    got = lax.all_to_all(sent, axis, 0, 0, tiled=True)
    return got.reshape((size * x.shape[0],) + x.shape[1:])


def _sum_over(x, axes, size):
    sent = jnp.broadcast_to(x[None], (size,) + x.shape)
    return lax.all_to_all(sent, axes, 0, 0, tiled=True).sum(0)


def shards(precond, out_factors, in_factors, token_mask, seq_ids, query_ids):
    num_queries = precond.shape[0]
    rows = lax.axis_size("row")
    cols = lax.axis_size("cz") * lax.axis_size("cy") * lax.axis_size("cc")

    groups = lax.axis_size("cz") * lax.axis_size("cy")
    cores = lax.axis_size("cc")
    core = lax.axis_index("cc")
    same = _gather(out_factors, ("cz", "cy"), groups).reshape((groups, 1) + out_factors.shape)
    other = lax.ppermute(same, "cc", [(0, 1), (1, 0)])
    out_all = jnp.where(
        core == 0, jnp.concatenate([same, other], axis=1), jnp.concatenate([other, same], axis=1)
    ).reshape((-1, out_factors.shape[1]))
    in_all = _gather(in_factors, "row", rows)
    weight = token_mask.astype(jnp.float32)[:, None] * (
        seq_ids[:, None] == jnp.arange(SEQ, dtype=jnp.int32)[None, :]
    ).astype(jnp.float32)
    weighted = weight.T.astype(jnp.bfloat16)[:, :, None] * out_all[None]
    grad = jnp.einsum("sti,tj->sij", weighted, in_all, preferred_element_type=jnp.float32)
    partial = jnp.sum(precond[:, None] * grad[None], axis=(2, 3))

    near = rows * cores * lax.axis_size("cy")
    summed = _sum_over(_sum_over(partial, ("row", "cy", "cc"), near), "cz", lax.axis_size("cz"))

    select = (query_ids[:, None] == jnp.arange(num_queries, dtype=jnp.int32)[None, :]).astype(
        jnp.float32
    )
    scale = 1.0 / math.sqrt(DOUT * DIN * LEN)
    return jnp.dot(select, summed, precision=lax.Precision.HIGHEST) * scale


def solution(mesh):
    rows, cols = mesh.devices.shape
    split = Mesh(mesh.devices.reshape(rows, cols // 4, 2, 2), ("row", "cz", "cy", "cc"))
    col = ("cz", "cy", "cc")
    placed = (P(None, "row", col), P(col, "row"), P("row", col), P(), P(), P())
    return jax.shard_map(shards, mesh=split, in_specs=placed, out_specs=P(), check_vma=False)
```

```python
import math

import jax
import jax.numpy as jnp
from jax import lax
from jax.sharding import Mesh, PartitionSpec as P

DOUT = 8192
DIN = 8192
SEQ = 4
LEN = 384
GATHER = "a2a"


def _gather(x, axis, size):
    if GATHER == "ag":
        return lax.all_gather(x, axis, axis=0, tiled=True)
    sent = jnp.broadcast_to(x[None], (size,) + x.shape)
    got = lax.all_to_all(sent, axis, 0, 0, tiled=True)
    return got.reshape((size * x.shape[0],) + x.shape[1:])


def _sum_over(x, axes, size):
    sent = jnp.broadcast_to(x[None], (size,) + x.shape)
    return lax.all_to_all(sent, axes, 0, 0, tiled=True).sum(0)


def shards(precond, out_factors, in_factors, token_mask, seq_ids, query_ids):
    num_queries = precond.shape[0]
    rows = lax.axis_size("row")
    cols = lax.axis_size("cz") * lax.axis_size("cy") * lax.axis_size("cc")

    groups = lax.axis_size("cz") * lax.axis_size("cy")
    cores = lax.axis_size("cc")
    core = lax.axis_index("cc")
    same = _gather(out_factors, ("cz", "cy"), groups).reshape((groups, 1) + out_factors.shape)
    other = lax.ppermute(same, "cc", [(0, 1), (1, 0)])
    out_all = jnp.where(
        core == 0, jnp.concatenate([same, other], axis=1), jnp.concatenate([other, same], axis=1)
    ).reshape((-1, out_factors.shape[1]))
    in_all = _gather(in_factors, "row", rows)
    weight = token_mask.astype(jnp.float32)[:, None] * (
        seq_ids[:, None] == jnp.arange(SEQ, dtype=jnp.int32)[None, :]
    ).astype(jnp.float32)
    weighted = weight.T.astype(jnp.bfloat16)[:, :, None] * out_all[None]
    grad = jnp.einsum("sti,tj->sij", weighted, in_all, preferred_element_type=jnp.float32)
    partial = jnp.sum(precond[:, None] * grad[None], axis=(2, 3))

    near = rows * cores * lax.axis_size("cy")
    summed = _sum_over(_sum_over(partial, ("row", "cy", "cc"), near), "cz", lax.axis_size("cz"))

    scale = 1.0 / math.sqrt(DOUT * DIN * LEN)
    return jnp.take(summed, query_ids, axis=0) * scale


def solution(mesh):
    rows, cols = mesh.devices.shape
    split = Mesh(mesh.devices.reshape(rows, cols // 4, 2, 2), ("row", "cz", "cy", "cc"))
    col = ("cz", "cy", "cc")
    placed = (P(None, "row", col), P(col, "row"), P("row", col), P(), P(), P())
    return jax.shard_map(shards, mesh=split, in_specs=placed, out_specs=P(), check_vma=False)
```
